128 devices in a mesh: expert: 32 (over x_lo, z, y), replica: 4 (over x_hi, core).
Axes of the slice: x: 4 (x_hi: 2, x_lo: 2; x = x_hi * 2 + x_lo), y: 4, z: 4, core: 2. Of those that a mesh axis runs over, the one named last changes fastest.
Arguments:
- tokens: bfloat16 [32768, 7168], P(('expert', 'replica')), may hold values from -6 to 6
- routes: int32 [32768, 8], P(('expert', 'replica')), may hold values from 0 to 255, all different within a row
- counts: int32 [128], P(('expert', 'replica')), may hold values from 128 to 256, as said below
- w_gate: bfloat16 [32, 7168, 2048], P('expert', None, 'replica'), may hold values from -0.0625 to 0.0625
- w_up: bfloat16 [32, 7168, 2048], P('expert', None, 'replica'), may hold values from -0.0625 to 0.0625
Outputs:
- key_cov: float32 [32, 2048, 2048], P('expert', 'replica')
The draws below stay inside these ranges and needn't reach their ends.
Inputs may be any that keep to these rules, and one draw needn't show every extreme that they name: `counts`: every count is a multiple of 128; some device has 256 and some 128.
All inputs are finite; a program needn't handle non-finite values.
Results may differ from the reference program's by a relative error of at most 0.0039.
Values may be sent and summed in bfloat16 or wider, within the bound.
No kernel may reach another device: no remote copies, remote signals or barrier semaphores. Data moves between devices by JAX's collectives and lax.ppermute only.
A program may use at most 128 MiB of HBM per device.

```python
import jax
import jax.numpy as jnp
from jax import lax

D = 7168
FF = 2048
N_ROUTED = 256
TOP = 8
TOK_DEV = 256
TOKENS = 32768
EXPERTS = 32
CAP = 8
SLOTS = 256
N_EXPERT = 32
N_REPLICA = 4


def draw_counts(key, part):
    device_total = N_EXPERT * N_REPLICA
    block_total = TOK_DEV // 128
    first_key, second_key = jax.random.split(jax.random.fold_in(key, 17))
    values = jax.random.randint(first_key, (device_total,), 1, block_total + 1) * 128
    chosen = jax.random.randint(second_key, (), 0, device_total)
    position = jnp.arange(device_total)
    values = jnp.where(position == chosen, TOK_DEV, values)
    values = jnp.where(position == (chosen + 1) % device_total, 128, values)
    return values.astype(jnp.int32)


def block_scale(own_key, shape, cuts, low, high):
    def one(dim, parts):
        draws = jax.random.uniform(jax.random.fold_in(jax.random.fold_in(own_key, 6), dim), (parts,), jnp.float32, low / len(cuts), high / len(cuts))
        return jnp.repeat(jnp.exp(draws), shape[dim] // parts).reshape((-1,) + (1,) * (len(shape) - dim - 1))

    loudness = one(*cuts[0])
    for cut in cuts[1:]:
        loudness = loudness * one(*cut)
    return loudness


def choose_distinct(key, rows, number_of, top, lift):
    sequence = jax.random.permutation(jax.random.fold_in(key, 1), number_of)
    pull = sequence
    for power in range(3):
        pull = pull * pull // number_of
    pull = pull * lift // number_of
    lots = jax.random.randint(jax.random.fold_in(key, 2), (rows, number_of), 0, 4096) + pull
    sure = jax.random.permutation(jax.random.fold_in(key, 3), rows)[jnp.arange(number_of) % rows]
    lots = jnp.where(jnp.arange(rows)[:, None] == sure[None, :], 1 << 14, lots)
    score = lots * number_of + jnp.arange(number_of)
    return lax.top_k(score.astype(jnp.int32), top)[1].astype(jnp.int32)


def normal_values(own_key, extent, spread, limit, shards=(), kind=jnp.bfloat16):
    drawn = jax.random.normal(own_key, extent, jnp.float32) * spread
    if len(shards) > 0:
        drawn = block_scale(own_key, extent, shards, -0.22, 0.18) * drawn
    return jnp.clip(drawn, min=-limit, max=limit).astype(kind)


def setup_inputs(seed: int = 0) -> dict:
    seeds = jax.random.split(jax.random.key(seed), 6)
    return {
        "tokens": normal_values(seeds[0], (TOKENS, D), 1.0, 6.0, ((0, 128),)),
        "routes": choose_distinct(seeds[1], TOKENS, N_ROUTED, TOP, 512),
        "counts": draw_counts(jax.random.fold_in(seeds[5], 71), 0),
        "w_gate": normal_values(seeds[3], (EXPERTS, D, FF), D ** -0.5, 0.0625, ((0, 32), (2, 4))),
        "w_up": normal_values(seeds[4], (EXPERTS, D, FF), D ** -0.5, 0.0625, ((0, 32), (2, 4))),
    }


def slot_tokens(route_block, real_count, expert_total, capacity):
    flat_route = route_block.reshape(-1)
    position = jnp.arange(flat_route.shape[0], dtype=jnp.int32)
    owner_token = position // TOP
    usable = (owner_token < real_count) & (flat_route < expert_total)
    hit_table = ((flat_route[:, None] == jnp.arange(expert_total, dtype=jnp.int32)[None, :]) & usable[:, None]).astype(jnp.int32)
    slot_rank = jnp.sum((jnp.cumsum(hit_table, axis=0) - hit_table) * hit_table, axis=1)
    kept_slot = usable & (slot_rank < capacity)
    slot_index = flat_route * capacity + slot_rank
    slot_match = kept_slot[:, None] & (slot_index[:, None] == jnp.arange(expert_total * capacity, dtype=jnp.int32)[None, :])
    filled = jnp.any(slot_match, axis=0)
    source = jnp.sum(jnp.where(slot_match, owner_token[:, None], 0), axis=0).astype(jnp.int32)
    return source, filled


def reference(tokens, routes, counts, w_gate, w_up):
    device_total = N_EXPERT * N_REPLICA
    route_blocks = routes.reshape(device_total, TOK_DEV, TOP)

    def per_device(items):
        return slot_tokens(items[0], items[1], EXPERTS, CAP)

    source, filled = lax.map(per_device, (route_blocks, counts))
    shifted = source + (jnp.arange(device_total, dtype=jnp.int32) * TOK_DEV)[:, None]
    row_index = shifted.reshape(device_total, EXPERTS, CAP).transpose(1, 0, 2).reshape(EXPERTS, device_total * CAP).astype(jnp.int32)
    row_live = filled.reshape(device_total, EXPERTS, CAP).transpose(1, 0, 2).reshape(EXPERTS, device_total * CAP)
    factor = 1.0 / SLOTS

    def per_expert(items):
        index_rows, live_rows, gate_matrix, up_matrix = items
        slot_rows = jnp.where(live_rows[:, None], tokens[index_rows], jnp.zeros((), tokens.dtype))
        gate_pre = jnp.dot(slot_rows, gate_matrix, preferred_element_type=jnp.float32)
        up_pre = jnp.dot(slot_rows, up_matrix, preferred_element_type=jnp.float32)
        keys = (jax.nn.silu(gate_pre) * up_pre).astype(jnp.bfloat16)
        return jnp.einsum("rf,rg->fg", keys, keys, preferred_element_type=jnp.float32) * factor

    return lax.map(per_expert, (row_index, row_live, w_gate, w_up))
```

```python
import jax
import jax.numpy as jnp
from jax import lax
from jax.sharding import Mesh, NamedSharding, PartitionSpec as P

N_ROUTED = 256
TOP = 8


def slot_onehot(routes, real_count, expert_total, capacity):
    tokens_here = routes.shape[0]
    token = lax.broadcasted_iota(jnp.int32, (tokens_here, 1), 0)
    expert = lax.broadcasted_iota(jnp.int32, (1, 1, expert_total), 2)
    hit = jnp.any(routes[:, :, None] == expert, axis=1) & (token < real_count)
    row = lax.broadcasted_iota(jnp.int32, (tokens_here, tokens_here), 0)
    col = lax.broadcasted_iota(jnp.int32, (tokens_here, tokens_here), 1)
    earlier = (col < row).astype(jnp.bfloat16)
    rank = jnp.dot(earlier, hit.astype(jnp.bfloat16), preferred_element_type=jnp.float32)
    rank = rank.astype(jnp.int32)
    slot = lax.broadcasted_iota(jnp.int32, (1, capacity, 1), 1)
    return hit.T[:, None, :] & (rank.T[:, None, :] == slot)


def body(tokens, routes, counts, w_gate, w_up):
    expert_count = lax.axis_size("expert")
    half_count = lax.axis_size("xh")
    core_count = lax.axis_size("core")
    slot_total, width_model = tokens.shape
    capacity = slot_total * TOP // N_ROUTED
    onehot = slot_onehot(routes, counts[0], expert_count, capacity)
    onehot = jnp.broadcast_to(
        onehot[:, None], (expert_count, half_count, capacity, slot_total)
    ).reshape(expert_count * half_count * capacity, slot_total)
    slot_rows = jnp.dot(
        onehot.astype(tokens.dtype), tokens, preferred_element_type=jnp.float32
    ).astype(tokens.dtype)
    slot_rows = slot_rows.reshape(expert_count * half_count, capacity, width_model)
    slot_block = lax.all_to_all(
        slot_rows, ("expert", "xh"), split_axis=0, concat_axis=0, tiled=True
    )
    slot_block = slot_block.reshape(expert_count * half_count * capacity, width_model)
    slot_block = lax.all_gather(slot_block, "core", axis=0, tiled=True)
    gate_pre = jnp.dot(slot_block, w_gate[0], preferred_element_type=jnp.float32)
    up_pre = jnp.dot(slot_block, w_up[0], preferred_element_type=jnp.float32)
    own_keys = (jax.nn.silu(gate_pre) * up_pre).astype(jnp.bfloat16)
    factor = 1.0 / (expert_count * capacity)
    key_gram = (
        jnp.einsum(
            "rf,rg->fg",
            own_keys,
            lax.all_gather(own_keys, ("xh", "core"), axis=1, tiled=True),
            preferred_element_type=jnp.float32,
        )
        * factor
    )
    return key_gram[None]


def solution(mesh):
    expert_count, replica_count = mesh.devices.shape
    split = Mesh(
        mesh.devices.reshape(expert_count, 2, replica_count // 2), ("expert", "xh", "core")
    )
    rows = ("expert", "xh", "core")
    step = jax.shard_map(
        body,
        mesh=split,
        in_specs=(
            P(rows, None),
            P(rows, None),
            P(rows),
            P("expert", None, ("xh", "core")),
            P("expert", None, ("xh", "core")),
        ),
        out_specs=P("expert", ("xh", "core"), None),
        check_vma=False,
    )
    out_sharding = NamedSharding(mesh, P("expert", "replica", None))

    def run(tokens, routes, counts, w_gate, w_up):
        out = step(tokens, routes, counts, w_gate, w_up)
        return lax.with_sharding_constraint(out, out_sharding)

    return run
```

```python
import jax
import jax.numpy as jnp
from jax import lax
from jax.sharding import Mesh, NamedSharding, PartitionSpec as P

N_ROUTED = 256
TOP = 8


def slot_onehot(routes, real_count, expert_total, capacity):
    tokens_here = routes.shape[0]
    token = lax.broadcasted_iota(jnp.int32, (tokens_here, 1), 0)
    expert = lax.broadcasted_iota(jnp.int32, (1, 1, expert_total), 2)
    hit = jnp.any(routes[:, :, None] == expert, axis=1) & (token < real_count)
    row = lax.broadcasted_iota(jnp.int32, (tokens_here, tokens_here), 0)
    col = lax.broadcasted_iota(jnp.int32, (tokens_here, tokens_here), 1)
    earlier = (col < row).astype(jnp.bfloat16)
    rank = jnp.dot(earlier, hit.astype(jnp.bfloat16), preferred_element_type=jnp.float32)
    rank = rank.astype(jnp.int32)
    slot = lax.broadcasted_iota(jnp.int32, (1, capacity, 1), 1)
    return hit.T[:, None, :] & (rank.T[:, None, :] == slot)


def body(tokens, routes, counts, w_gate, w_up):
    expert_count = lax.axis_size("expert")
    half_count = lax.axis_size("xh")
    core_count = lax.axis_size("core")
    slot_total, width_model = tokens.shape
    capacity = slot_total * TOP // N_ROUTED
    onehot = slot_onehot(routes, counts[0], expert_count, capacity)
    onehot = jnp.broadcast_to(
        onehot[:, None], (expert_count, half_count, capacity, slot_total)
    ).reshape(expert_count * half_count * capacity, slot_total)
    slot_rows = jnp.dot(
        onehot.astype(tokens.dtype), tokens, preferred_element_type=jnp.float32
    ).astype(tokens.dtype)
    slot_rows = slot_rows.reshape(expert_count * half_count, capacity, width_model)
    slot_block = lax.all_to_all(
        slot_rows, ("expert", "xh"), split_axis=0, concat_axis=0, tiled=True
    )
    slot_block = slot_block.reshape(expert_count * half_count * capacity, width_model)
    partner = lax.ppermute(slot_block, "core", [(c, (c + 1) % core_count) for c in range(core_count)])
    factor = 1.0 / (expert_count * capacity)
    own_keys, gathered = [], []
    for rows in (slot_block, partner):
        gate_pre = jnp.dot(rows, w_gate[0], preferred_element_type=jnp.float32)
        up_pre = jnp.dot(rows, w_up[0], preferred_element_type=jnp.float32)
        keys = (jax.nn.silu(gate_pre) * up_pre).astype(jnp.bfloat16)
        own_keys.append(keys)
        gathered.append(lax.all_gather(keys, ("xh", "core"), axis=0))
    first_core = lax.axis_index("core") == 0
    from_core = (
        jnp.where(first_core, own_keys[0], own_keys[1]),
        jnp.where(first_core, own_keys[1], own_keys[0]),
    )
    blocks = []
    for replica in range(half_count * core_count):
        source = replica % core_count
        block = jnp.dot(
            from_core[source].T, gathered[0][replica], preferred_element_type=jnp.float32
        ) + jnp.dot(
            from_core[1 - source].T, gathered[1][replica], preferred_element_type=jnp.float32
        )
        blocks.append(block)
    key_gram = jnp.concatenate(blocks, axis=1) * factor
    return key_gram[None]


def solution(mesh):
    expert_count, replica_count = mesh.devices.shape
    split = Mesh(
        mesh.devices.reshape(expert_count, 2, replica_count // 2), ("expert", "xh", "core")
    )
    rows = ("expert", "xh", "core")
    step = jax.shard_map(
        body,
        mesh=split,
        in_specs=(
            P(rows, None),
            P(rows, None),
            P(rows),
            P("expert", None, ("xh", "core")),
            P("expert", None, ("xh", "core")),
        ),
        out_specs=P("expert", ("xh", "core"), None),
        check_vma=False,
    )
    out_sharding = NamedSharding(mesh, P("expert", "replica", None))

    def run(tokens, routes, counts, w_gate, w_up):
        out = step(tokens, routes, counts, w_gate, w_up)
        return lax.with_sharding_constraint(out, out_sharding)

    return run
```

```python
import jax
import jax.numpy as jnp
from jax import lax
from jax.sharding import Mesh, NamedSharding, PartitionSpec as P

N_ROUTED = 256
TOP = 8


def slot_onehot(routes, real_count, expert_total, capacity):
    tokens_here = routes.shape[0]
    token = lax.broadcasted_iota(jnp.int32, (tokens_here, 1), 0)
    expert = lax.broadcasted_iota(jnp.int32, (1, 1, expert_total), 2)
    hit = jnp.any(routes[:, :, None] == expert, axis=1) & (token < real_count)
    row = lax.broadcasted_iota(jnp.int32, (tokens_here, tokens_here), 0)
    col = lax.broadcasted_iota(jnp.int32, (tokens_here, tokens_here), 1)
    earlier = (col < row).astype(jnp.bfloat16)
    rank = jnp.dot(earlier, hit.astype(jnp.bfloat16), preferred_element_type=jnp.float32)
    rank = rank.astype(jnp.int32)
    slot = lax.broadcasted_iota(jnp.int32, (1, capacity, 1), 1)
    return hit.T[:, None, :] & (rank.T[:, None, :] == slot)


def body(tokens, routes, counts, w_gate, w_up):
    expert_count = lax.axis_size("expert")
    half_count = lax.axis_size("xh")
    core_count = lax.axis_size("core")
    slot_total, width_model = tokens.shape
    capacity = slot_total * TOP // N_ROUTED
    onehot = slot_onehot(routes, counts[0], expert_count, capacity)
    onehot = jnp.broadcast_to(
        onehot[:, None], (expert_count, half_count, capacity, slot_total)
    ).reshape(expert_count * half_count * capacity, slot_total)
    slot_rows = jnp.dot(
        onehot.astype(tokens.dtype), tokens, preferred_element_type=jnp.float32
    ).astype(tokens.dtype)
    slot_rows = slot_rows.reshape(expert_count * half_count, capacity, width_model)
    slot_block = lax.all_to_all(
        slot_rows, ("expert", "xh"), split_axis=0, concat_axis=0, tiled=True
    )
    slot_block = slot_block.reshape(expert_count * half_count * capacity, width_model)
    partner = lax.ppermute(slot_block, "core", [(c, (c + 1) % core_count) for c in range(core_count)])
    factor = 1.0 / (expert_count * capacity)
    swap_half = [(h, (h + 1) % half_count) for h in range(half_count)]
    swap_core = [(c, (c + 1) % core_count) for c in range(core_count)]
    replica_count = half_count * core_count
    swap_both = [(r, r ^ (replica_count - 1)) for r in range(replica_count)]
    blocks = [[None] * 4, [None] * 4]
    for i, rows in enumerate((slot_block, partner)):
        gate_pre = jnp.dot(rows, w_gate[0], preferred_element_type=jnp.float32)
        up_pre = jnp.dot(rows, w_up[0], preferred_element_type=jnp.float32)
        keys = (jax.nn.silu(gate_pre) * up_pre).astype(jnp.bfloat16)
        blocks[i][0] = keys
        blocks[i][2] = lax.ppermute(keys, "xh", swap_half)
        blocks[1 - i][1] = lax.ppermute(keys, "core", swap_core)
        blocks[1 - i][3] = lax.ppermute(keys, ("xh", "core"), swap_both)
    on_second_core = lax.axis_index("core") == 1
    on_second_half = lax.axis_index("xh") == 1

    def absolute(rel):
        by_core = [jnp.where(on_second_core, rel[k ^ 1], rel[k]) for k in range(4)]
        by_half = [jnp.where(on_second_half, by_core[k ^ 2], by_core[k]) for k in range(4)]
        return jnp.concatenate(by_half, axis=1)

    key_gram = None
    for i in range(2):
        part = jnp.einsum(
            "rf,rg->fg", blocks[i][0], absolute(blocks[i]), preferred_element_type=jnp.float32
        )
        key_gram = part if key_gram is None else key_gram + part
    key_gram = key_gram * factor
    return key_gram[None]


def solution(mesh):
    expert_count, replica_count = mesh.devices.shape
    split = Mesh(
        mesh.devices.reshape(expert_count, 2, replica_count // 2), ("expert", "xh", "core")
    )
    rows = ("expert", "xh", "core")
    step = jax.shard_map(
        body,
        mesh=split,
        in_specs=(
            P(rows, None),
            P(rows, None),
            P(rows),
            P("expert", None, ("xh", "core")),
            P("expert", None, ("xh", "core")),
        ),
        out_specs=P("expert", ("xh", "core"), None),
        check_vma=False,
    )
    out_sharding = NamedSharding(mesh, P("expert", "replica", None))

    def run(tokens, routes, counts, w_gate, w_up):
        out = step(tokens, routes, counts, w_gate, w_up)
        return lax.with_sharding_constraint(out, out_sharding)

    return run
```

```python
import jax
import jax.numpy as jnp
from jax import lax
from jax.sharding import Mesh, NamedSharding, PartitionSpec as P

N_ROUTED = 256
TOP = 8
CHUNKS = 2


def slot_onehot(routes, real_count, expert_total, capacity):
    tokens_here = routes.shape[0]
    token = lax.broadcasted_iota(jnp.int32, (tokens_here, 1), 0)
    expert = lax.broadcasted_iota(jnp.int32, (1, 1, expert_total), 2)
    hit = jnp.any(routes[:, :, None] == expert, axis=1) & (token < real_count)
    row = lax.broadcasted_iota(jnp.int32, (tokens_here, tokens_here), 0)
    col = lax.broadcasted_iota(jnp.int32, (tokens_here, tokens_here), 1)
    earlier = (col < row).astype(jnp.bfloat16)
    rank = jnp.dot(earlier, hit.astype(jnp.bfloat16), preferred_element_type=jnp.float32)
    rank = rank.astype(jnp.int32)
    slot = lax.broadcasted_iota(jnp.int32, (1, capacity, 1), 1)
    return hit.T[:, None, :] & (rank.T[:, None, :] == slot)


def body(tokens, routes, counts, w_gate, w_up):
    expert_count = lax.axis_size("expert")
    half_count = lax.axis_size("xh")
    core_count = lax.axis_size("core")
    slot_total, width_model = tokens.shape
    capacity = slot_total * TOP // N_ROUTED
    onehot = slot_onehot(routes, counts[0], expert_count, capacity)
    onehot = jnp.broadcast_to(
        onehot[:, None], (expert_count, half_count, capacity, slot_total)
    ).reshape(expert_count * half_count * capacity, slot_total)
    slot_rows = jnp.dot(
        onehot.astype(tokens.dtype), tokens, preferred_element_type=jnp.float32
    ).astype(tokens.dtype)
    slot_rows = slot_rows.reshape(expert_count * half_count, capacity, width_model)
    factor = 1.0 / (expert_count * capacity)
    swap_half = [(h, (h + 1) % half_count) for h in range(half_count)]
    swap_core = [(c, (c + 1) % core_count) for c in range(core_count)]
    replica_count = half_count * core_count
    swap_both = [(r, r ^ (replica_count - 1)) for r in range(replica_count)]
    per_chunk = capacity // CHUNKS
    own = []
    for q in range(CHUNKS):
        piece = lax.all_to_all(
            slot_rows[:, q * per_chunk:(q + 1) * per_chunk], ("expert", "xh"),
            split_axis=0, concat_axis=0, tiled=True,
        )
        own.append(piece.reshape(expert_count * half_count * per_chunk, width_model))
    partner = [lax.ppermute(piece, "core", swap_core) for piece in own]
    blocks = {(q, s): [None] * 4 for q in range(CHUNKS) for s in range(2)}
    work = [(q, 0, own[q]) for q in range(CHUNKS)] + [(q, 1, partner[q]) for q in range(CHUNKS)]
    for q, s, rows in work:
        gate_pre = jnp.dot(rows, w_gate[0], preferred_element_type=jnp.float32)
        up_pre = jnp.dot(rows, w_up[0], preferred_element_type=jnp.float32)
        keys = (jax.nn.silu(gate_pre) * up_pre).astype(jnp.bfloat16)
        blocks[(q, s)][0] = keys
        blocks[(q, s)][2] = lax.ppermute(keys, "xh", swap_half)
        blocks[(q, 1 - s)][1] = lax.ppermute(keys, "core", swap_core)
        blocks[(q, 1 - s)][3] = lax.ppermute(keys, ("xh", "core"), swap_both)
    on_second_core = lax.axis_index("core") == 1
    on_second_half = lax.axis_index("xh") == 1

    def absolute(rel):
        by_core = [jnp.where(on_second_core, rel[k ^ 1], rel[k]) for k in range(4)]
        by_half = [jnp.where(on_second_half, by_core[k ^ 2], by_core[k]) for k in range(4)]
        return jnp.concatenate(by_half, axis=1)

    key_gram = None
    for q, s, _ in work:
        part = jnp.einsum(
            "rf,rg->fg", blocks[(q, s)][0], absolute(blocks[(q, s)]),
            preferred_element_type=jnp.float32,
        )
        key_gram = part if key_gram is None else key_gram + part
    key_gram = key_gram * factor
    return key_gram[None]


def solution(mesh):
    expert_count, replica_count = mesh.devices.shape
    split = Mesh(
        mesh.devices.reshape(expert_count, 2, replica_count // 2), ("expert", "xh", "core")
    )
    rows = ("expert", "xh", "core")
    step = jax.shard_map(
        body,
        mesh=split,
        in_specs=(
            P(rows, None),
            P(rows, None),
            P(rows),
            P("expert", None, ("xh", "core")),
            P("expert", None, ("xh", "core")),
        ),
        out_specs=P("expert", ("xh", "core"), None),
        check_vma=False,
    )
    out_sharding = NamedSharding(mesh, P("expert", "replica", None))

    def run(tokens, routes, counts, w_gate, w_up):
        out = step(tokens, routes, counts, w_gate, w_up)
        return lax.with_sharding_constraint(out, out_sharding)

    return run
```

```python
import jax
import jax.numpy as jnp
from jax import lax
from jax.sharding import Mesh, NamedSharding, PartitionSpec as P

N_ROUTED = 256
TOP = 8


def slot_onehot(routes, real_count, expert_total, capacity):
    tokens_here = routes.shape[0]
    token = lax.broadcasted_iota(jnp.int32, (tokens_here, 1), 0)
    expert = lax.broadcasted_iota(jnp.int32, (1, 1, expert_total), 2)
    hit = jnp.any(routes[:, :, None] == expert, axis=1) & (token < real_count)
    row = lax.broadcasted_iota(jnp.int32, (tokens_here, tokens_here), 0)
    col = lax.broadcasted_iota(jnp.int32, (tokens_here, tokens_here), 1)
    earlier = (col < row).astype(jnp.bfloat16)
    rank = jnp.dot(earlier, hit.astype(jnp.bfloat16), preferred_element_type=jnp.float32)
    rank = rank.astype(jnp.int32)
    slot = lax.broadcasted_iota(jnp.int32, (1, capacity, 1), 1)
    return hit.T[:, None, :] & (rank.T[:, None, :] == slot)


def body(tokens, routes, counts, w_gate, w_up):
    expert_count = lax.axis_size("expert")
    half_count = lax.axis_size("xh")
    core_count = lax.axis_size("core")
    slot_total, width_model = tokens.shape
    capacity = slot_total * TOP // N_ROUTED
    onehot = slot_onehot(routes, counts[0], expert_count, capacity)
    onehot = jnp.broadcast_to(
        onehot[:, None], (expert_count, half_count, capacity, slot_total)
    ).reshape(expert_count * half_count * capacity, slot_total)
    slot_rows = jnp.dot(
        onehot.astype(tokens.dtype), tokens, preferred_element_type=jnp.float32
    ).astype(tokens.dtype)
    slot_rows = slot_rows.reshape(expert_count * half_count, capacity, width_model)
    slot_block = lax.all_to_all(
        slot_rows, ("expert", "xh"), split_axis=0, concat_axis=0, tiled=True
    )
    slot_block = slot_block.reshape(expert_count * half_count * capacity, width_model)
    partner = lax.ppermute(slot_block, "core", [(c, (c + 1) % core_count) for c in range(core_count)])
    factor = 1.0 / (expert_count * capacity)
    replica_count = half_count * core_count
    halves = []
    for rows in (slot_block, partner):
        gate_pre = jnp.dot(rows, w_gate[0], preferred_element_type=jnp.float32)
        up_pre = jnp.dot(rows, w_up[0], preferred_element_type=jnp.float32)
        halves.append((jax.nn.silu(gate_pre) * up_pre).astype(jnp.bfloat16))
    in_order = jnp.concatenate(halves, axis=0)
    swapped = jnp.concatenate(halves[::-1], axis=0)
    canonical = jnp.where(lax.axis_index("core") == 0, in_order, swapped)
    sent = jnp.broadcast_to(in_order[None], (replica_count,) + in_order.shape)
    received = lax.all_to_all(sent, ("xh", "core"), split_axis=0, concat_axis=0, tiled=True)
    rows_half = in_order.shape[0] // 2
    columns = []
    for replica in range(replica_count):
        block = received[replica]
        if replica % core_count == 1:
            block = jnp.concatenate([block[rows_half:], block[:rows_half]], axis=0)
        columns.append(block)
    every = jnp.concatenate(columns, axis=1)
    key_gram = (
        jnp.einsum("rf,rg->fg", canonical, every, preferred_element_type=jnp.float32) * factor
    )
    return key_gram[None]


def solution(mesh):
    expert_count, replica_count = mesh.devices.shape
    split = Mesh(
        mesh.devices.reshape(expert_count, 2, replica_count // 2), ("expert", "xh", "core")
    )
    rows = ("expert", "xh", "core")
    step = jax.shard_map(
        body,
        mesh=split,
        in_specs=(
            P(rows, None),
            P(rows, None),
            P(rows),
            P("expert", None, ("xh", "core")),
            P("expert", None, ("xh", "core")),
        ),
        out_specs=P("expert", ("xh", "core"), None),
        check_vma=False,
    )
    out_sharding = NamedSharding(mesh, P("expert", "replica", None))

    def run(tokens, routes, counts, w_gate, w_up):
        out = step(tokens, routes, counts, w_gate, w_up)
        return lax.with_sharding_constraint(out, out_sharding)

    return run
```

```python
import jax
import jax.numpy as jnp
from jax import lax
from jax.experimental.layout import Layout, with_layout_constraint
from jax.sharding import Mesh, NamedSharding, PartitionSpec as P

N_ROUTED = 256
TOP = 8


def slot_onehot(routes, real_count, expert_total, capacity):
    tokens_here = routes.shape[0]
    token = lax.broadcasted_iota(jnp.int32, (tokens_here, 1), 0)
    expert = lax.broadcasted_iota(jnp.int32, (1, 1, expert_total), 2)
    hit = jnp.any(routes[:, :, None] == expert, axis=1) & (token < real_count)
    row = lax.broadcasted_iota(jnp.int32, (tokens_here, tokens_here), 0)
    col = lax.broadcasted_iota(jnp.int32, (tokens_here, tokens_here), 1)
    earlier = (col < row).astype(jnp.bfloat16)
    rank = jnp.dot(earlier, hit.astype(jnp.bfloat16), preferred_element_type=jnp.float32)
    rank = rank.astype(jnp.int32)
    slot = lax.broadcasted_iota(jnp.int32, (1, capacity, 1), 1)
    return hit.T[:, None, :] & (rank.T[:, None, :] == slot)


def body(tokens, routes, counts, w_gate, w_up):
    expert_count = lax.axis_size("expert")
    half_count = lax.axis_size("xh")
    core_count = lax.axis_size("core")
    slot_total, width_model = tokens.shape
    capacity = slot_total * TOP // N_ROUTED
    onehot = slot_onehot(routes, counts[0], expert_count, capacity)
    onehot = jnp.broadcast_to(
        onehot[:, None], (expert_count, half_count, capacity, slot_total)
    ).reshape(expert_count * half_count * capacity, slot_total)
    slot_rows = jnp.dot(
        onehot.astype(tokens.dtype), tokens, preferred_element_type=jnp.float32
    ).astype(tokens.dtype)
    slot_rows = slot_rows.reshape(expert_count * half_count, capacity, width_model)
    slot_block = lax.all_to_all(
        slot_rows, ("expert", "xh"), split_axis=0, concat_axis=0, tiled=True
    )
    slot_block = slot_block.reshape(expert_count * half_count * capacity, width_model)
    partner = lax.ppermute(slot_block, "core", [(c, (c + 1) % core_count) for c in range(core_count)])
    factor = 1.0 / (expert_count * capacity)
    swap_half = [(h, (h + 1) % half_count) for h in range(half_count)]
    swap_core = [(c, (c + 1) % core_count) for c in range(core_count)]
    replica_count = half_count * core_count
    swap_both = [(r, r ^ (replica_count - 1)) for r in range(replica_count)]
    blocks = [[None] * 4, [None] * 4]
    for i, rows in enumerate((slot_block, partner)):
        gate_pre = jnp.dot(rows, w_gate[0], preferred_element_type=jnp.float32)
        up_pre = jnp.dot(rows, w_up[0], preferred_element_type=jnp.float32)
        keys = (jax.nn.silu(gate_pre) * up_pre).astype(jnp.bfloat16)
        keys = with_layout_constraint(keys, Layout(major_to_minor=(0, 1)))
        blocks[i][0] = keys
        blocks[i][2] = lax.ppermute(keys, "xh", swap_half)
        blocks[1 - i][1] = lax.ppermute(keys, "core", swap_core)
        blocks[1 - i][3] = lax.ppermute(keys, ("xh", "core"), swap_both)
    on_second_core = lax.axis_index("core") == 1
    on_second_half = lax.axis_index("xh") == 1

    def absolute(rel):
        by_core = [jnp.where(on_second_core, rel[k ^ 1], rel[k]) for k in range(4)]
        by_half = [jnp.where(on_second_half, by_core[k ^ 2], by_core[k]) for k in range(4)]
        return jnp.concatenate(by_half, axis=1)

    key_gram = None
    for i in range(2):
        part = jnp.einsum(
            "rf,rg->fg", blocks[i][0], absolute(blocks[i]), preferred_element_type=jnp.float32
        )
        key_gram = part if key_gram is None else key_gram + part
    key_gram = key_gram * factor
    return key_gram[None]


def solution(mesh):
    expert_count, replica_count = mesh.devices.shape
    split = Mesh(
        mesh.devices.reshape(expert_count, 2, replica_count // 2), ("expert", "xh", "core")
    )
    rows = ("expert", "xh", "core")
    step = jax.shard_map(
        body,
        mesh=split,
        in_specs=(
            P(rows, None),
            P(rows, None),
            P(rows),
            P("expert", None, ("xh", "core")),
            P("expert", None, ("xh", "core")),
        ),
        out_specs=P("expert", ("xh", "core"), None),
        check_vma=False,
    )
    out_sharding = NamedSharding(mesh, P("expert", "replica", None))

    def run(tokens, routes, counts, w_gate, w_up):
        out = step(tokens, routes, counts, w_gate, w_up)
        return lax.with_sharding_constraint(out, out_sharding)

    return run
```

```python
import jax
import jax.numpy as jnp
from jax import lax
from jax.experimental.layout import Layout, with_layout_constraint
from jax.sharding import Mesh, NamedSharding, PartitionSpec as P

N_ROUTED = 256
TOP = 8


def slot_onehot(routes, real_count, expert_total, capacity):
    tokens_here = routes.shape[0]
    token = lax.broadcasted_iota(jnp.int32, (tokens_here, 1), 0)
    expert = lax.broadcasted_iota(jnp.int32, (1, 1, expert_total), 2)
    hit = jnp.any(routes[:, :, None] == expert, axis=1) & (token < real_count)
    row = lax.broadcasted_iota(jnp.int32, (tokens_here, tokens_here), 0)
    col = lax.broadcasted_iota(jnp.int32, (tokens_here, tokens_here), 1)
    earlier = (col < row).astype(jnp.bfloat16)
    rank = jnp.dot(earlier, hit.astype(jnp.bfloat16), preferred_element_type=jnp.float32)
    rank = rank.astype(jnp.int32)
    slot = lax.broadcasted_iota(jnp.int32, (1, capacity, 1), 1)
    return hit.T[:, None, :] & (rank.T[:, None, :] == slot)


def body(tokens, routes, counts, w_gate, w_up):
    expert_count = lax.axis_size("expert")
    half_count = lax.axis_size("xh")
    core_count = lax.axis_size("core")
    slot_total, width_model = tokens.shape
    capacity = slot_total * TOP // N_ROUTED
    onehot = slot_onehot(routes, counts[0], expert_count, capacity)
    onehot = jnp.broadcast_to(
        onehot[:, None], (expert_count, half_count, capacity, slot_total)
    ).reshape(expert_count * half_count * capacity, slot_total)
    slot_rows = jnp.dot(
        onehot.astype(tokens.dtype), tokens, preferred_element_type=jnp.float32
    ).astype(tokens.dtype)
    slot_rows = slot_rows.reshape(expert_count * half_count, capacity, width_model)
    slot_block = lax.all_to_all(
        slot_rows, ("expert", "xh"), split_axis=0, concat_axis=0, tiled=True
    )
    slot_block = slot_block.reshape(expert_count * half_count * capacity, width_model)
    partner = lax.ppermute(slot_block, "core", [(c, (c + 1) % core_count) for c in range(core_count)])
    factor = 1.0 / (expert_count * capacity)
    swap_half = [(h, (h + 1) % half_count) for h in range(half_count)]
    swap_core = [(c, (c + 1) % core_count) for c in range(core_count)]
    replica_count = half_count * core_count
    own_keys, far_keys = [], []
    for rows in (slot_block, partner):
        gate_pre = jnp.dot(rows, w_gate[0], preferred_element_type=jnp.float32)
        up_pre = jnp.dot(rows, w_up[0], preferred_element_type=jnp.float32)
        keys = (jax.nn.silu(gate_pre) * up_pre).astype(jnp.bfloat16)
        keys = with_layout_constraint(keys, Layout(major_to_minor=(0, 1)))
        own_keys.append(keys)
        far_keys.append(lax.ppermute(keys, "xh", swap_half))
    relayed = lax.ppermute(jnp.stack(own_keys + far_keys), "core", swap_core)
    blocks = [
        [own_keys[i], relayed[1 - i], far_keys[i], relayed[3 - i]] for i in range(2)
    ]
    on_second_core = lax.axis_index("core") == 1
    on_second_half = lax.axis_index("xh") == 1

    def absolute(rel):
        by_core = [jnp.where(on_second_core, rel[k ^ 1], rel[k]) for k in range(4)]
        by_half = [jnp.where(on_second_half, by_core[k ^ 2], by_core[k]) for k in range(4)]
        return jnp.concatenate(by_half, axis=1)

    key_gram = None
    for i in range(2):
        part = jnp.einsum(
            "rf,rg->fg", blocks[i][0], absolute(blocks[i]), preferred_element_type=jnp.float32
        )
        key_gram = part if key_gram is None else key_gram + part
    key_gram = key_gram * factor
    return key_gram[None]


def solution(mesh):
    expert_count, replica_count = mesh.devices.shape
    split = Mesh(
        mesh.devices.reshape(expert_count, 2, replica_count // 2), ("expert", "xh", "core")
    )
    rows = ("expert", "xh", "core")
    step = jax.shard_map(
        body,
        mesh=split,
        in_specs=(
            P(rows, None),
            P(rows, None),
            P(rows),
            P("expert", None, ("xh", "core")),
            P("expert", None, ("xh", "core")),
        ),
        out_specs=P("expert", ("xh", "core"), None),
        check_vma=False,
    )
    out_sharding = NamedSharding(mesh, P("expert", "replica", None))

    def run(tokens, routes, counts, w_gate, w_up):
        out = step(tokens, routes, counts, w_gate, w_up)
        return lax.with_sharding_constraint(out, out_sharding)

    return run
```

```python
import jax
import jax.numpy as jnp
from jax import lax
from jax.experimental.layout import Layout, with_layout_constraint
from jax.sharding import Mesh, NamedSharding, PartitionSpec as P

N_ROUTED = 256
TOP = 8


def slot_onehot(routes, real_count, expert_total, capacity):
    tokens_here = routes.shape[0]
    token = lax.broadcasted_iota(jnp.int32, (tokens_here, 1), 0)
    expert = lax.broadcasted_iota(jnp.int32, (1, 1, expert_total), 2)
    hit = jnp.any(routes[:, :, None] == expert, axis=1) & (token < real_count)
    row = lax.broadcasted_iota(jnp.int32, (tokens_here, tokens_here), 0)
    col = lax.broadcasted_iota(jnp.int32, (tokens_here, tokens_here), 1)
    earlier = (col < row).astype(jnp.bfloat16)
    rank = jnp.dot(earlier, hit.astype(jnp.bfloat16), preferred_element_type=jnp.float32)
    rank = rank.astype(jnp.int32)
    slot = lax.broadcasted_iota(jnp.int32, (1, capacity, 1), 1)
    return hit.T[:, None, :] & (rank.T[:, None, :] == slot)


def body(tokens, routes, counts, w_gate, w_up):
    expert_count = lax.axis_size("expert")
    half_count = lax.axis_size("xh")
    core_count = lax.axis_size("core")
    slot_total, width_model = tokens.shape
    capacity = slot_total * TOP // N_ROUTED
    onehot = slot_onehot(routes, counts[0], expert_count, capacity)
    onehot = jnp.broadcast_to(
        onehot[:, None], (expert_count, half_count, capacity, slot_total)
    ).reshape(expert_count * half_count * capacity, slot_total)
    slot_rows = jnp.dot(
        onehot.astype(tokens.dtype), tokens, preferred_element_type=jnp.float32
    ).astype(tokens.dtype)
    slot_rows = slot_rows.reshape(expert_count * half_count, capacity, width_model)
    slot_block = lax.all_to_all(
        slot_rows, ("expert", "xh"), split_axis=0, concat_axis=0, tiled=True
    )
    slot_block = slot_block.reshape(expert_count * half_count * capacity, width_model)
    partner = lax.ppermute(slot_block, "core", [(c, (c + 1) % core_count) for c in range(core_count)])
    factor = 1.0 / (expert_count * capacity)
    swap_half = [(h, (h + 1) % half_count) for h in range(half_count)]
    swap_core = [(c, (c + 1) % core_count) for c in range(core_count)]
    replica_count = half_count * core_count
    ring = half_count * 2
    expert_inner = expert_count // 2

    def step(shift):
        pairs = []
        for expert in range(expert_count):
            for half in range(half_count):
                x = half * 2 + expert // expert_inner
                moved = (x + shift) % ring
                target = (moved % 2) * expert_inner + expert % expert_inner
                pairs.append((expert * half_count + half, target * half_count + moved // 2))
        return pairs

    step_up, step_down = step(1), step(-1)
    own_keys, far_keys = [], []
    for rows in (slot_block, partner):
        gate_pre = jnp.dot(rows, w_gate[0], preferred_element_type=jnp.float32)
        up_pre = jnp.dot(rows, w_up[0], preferred_element_type=jnp.float32)
        keys = (jax.nn.silu(gate_pre) * up_pre).astype(jnp.bfloat16)
        keys = with_layout_constraint(keys, Layout(major_to_minor=(0, 1)))
        own_keys.append(keys)
        rows_half = keys.shape[0] // 2
        forward = keys[:rows_half]
        backward = keys[rows_half:]
        for _ in range(half_count):
            forward = lax.ppermute(forward, ("expert", "xh"), step_up)
            backward = lax.ppermute(backward, ("expert", "xh"), step_down)
        far_keys.append(jnp.concatenate([forward, backward], axis=0))
    relayed = lax.ppermute(jnp.stack(own_keys + far_keys), "core", swap_core)
    blocks = [
        [own_keys[i], relayed[1 - i], far_keys[i], relayed[3 - i]] for i in range(2)
    ]
    on_second_core = lax.axis_index("core") == 1
    on_second_half = lax.axis_index("xh") == 1

    def absolute(rel):
        by_core = [jnp.where(on_second_core, rel[k ^ 1], rel[k]) for k in range(4)]
        by_half = [jnp.where(on_second_half, by_core[k ^ 2], by_core[k]) for k in range(4)]
        return jnp.concatenate(by_half, axis=1)

    key_gram = None
    for i in range(2):
        part = jnp.einsum(
            "rf,rg->fg", blocks[i][0], absolute(blocks[i]), preferred_element_type=jnp.float32
        )
        key_gram = part if key_gram is None else key_gram + part
    key_gram = key_gram * factor
    return key_gram[None]


def solution(mesh):
    expert_count, replica_count = mesh.devices.shape
    split = Mesh(
        mesh.devices.reshape(expert_count, 2, replica_count // 2), ("expert", "xh", "core")
    )
    rows = ("expert", "xh", "core")
    step = jax.shard_map(
        body,
        mesh=split,
        in_specs=(
            P(rows, None),
            P(rows, None),
            P(rows),
            P("expert", None, ("xh", "core")),
            P("expert", None, ("xh", "core")),
        ),
        out_specs=P("expert", ("xh", "core"), None),
        check_vma=False,
    )
    out_sharding = NamedSharding(mesh, P("expert", "replica", None))

    def run(tokens, routes, counts, w_gate, w_up):
        out = step(tokens, routes, counts, w_gate, w_up)
        return lax.with_sharding_constraint(out, out_sharding)

    return run
```

```python
import jax
import jax.numpy as jnp
from jax import lax
from jax.experimental.layout import Layout, with_layout_constraint
from jax.sharding import Mesh, NamedSharding, PartitionSpec as P

N_ROUTED = 256
TOP = 8


def slot_onehot(routes, real_count, expert_total, capacity):
    tokens_here = routes.shape[0]
    token = lax.broadcasted_iota(jnp.int32, (tokens_here, 1), 0)
    expert = lax.broadcasted_iota(jnp.int32, (1, 1, expert_total), 2)
    hit = jnp.any(routes[:, :, None] == expert, axis=1) & (token < real_count)
    row = lax.broadcasted_iota(jnp.int32, (tokens_here, tokens_here), 0)
    col = lax.broadcasted_iota(jnp.int32, (tokens_here, tokens_here), 1)
    earlier = (col < row).astype(jnp.bfloat16)
    rank = jnp.dot(earlier, hit.astype(jnp.bfloat16), preferred_element_type=jnp.float32)
    rank = rank.astype(jnp.int32)
    slot = lax.broadcasted_iota(jnp.int32, (1, capacity, 1), 1)
    return hit.T[:, None, :] & (rank.T[:, None, :] == slot)


def body(tokens, routes, counts, w_gate, w_up):
    expert_count = lax.axis_size("expert")
    half_count = lax.axis_size("xh")
    core_count = lax.axis_size("core")
    slot_total, width_model = tokens.shape
    capacity = slot_total * TOP // N_ROUTED
    onehot = slot_onehot(routes, counts[0], expert_count, capacity)
    onehot = jnp.broadcast_to(
        onehot[:, None], (expert_count, half_count, capacity, slot_total)
    ).reshape(expert_count * half_count * capacity, slot_total)
    slot_rows = jnp.dot(
        onehot.astype(tokens.dtype), tokens, preferred_element_type=jnp.float32
    ).astype(tokens.dtype)
    slot_rows = slot_rows.reshape(expert_count * half_count, capacity, width_model)
    slot_block = lax.all_to_all(
        slot_rows, ("expert", "xh"), split_axis=0, concat_axis=0, tiled=True
    )
    slot_block = slot_block.reshape(expert_count * half_count * capacity, width_model)
    partner = lax.ppermute(slot_block, "core", [(c, (c + 1) % core_count) for c in range(core_count)])
    factor = 1.0 / (expert_count * capacity)
    swap_half = [(h, (h + 1) % half_count) for h in range(half_count)]
    swap_core = [(c, (c + 1) % core_count) for c in range(core_count)]
    replica_count = half_count * core_count
    own_keys, far_keys = [], []
    for rows in (slot_block, partner):
        gate_pre = jnp.dot(rows, w_gate[0], preferred_element_type=jnp.float32)
        up_pre = jnp.dot(rows, w_up[0], preferred_element_type=jnp.float32)
        keys = (jax.nn.silu(gate_pre) * up_pre).astype(jnp.bfloat16)
        keys = with_layout_constraint(keys, Layout(major_to_minor=(0, 1)))
        own_keys.append(keys)
        far_keys.append(lax.ppermute(keys, "xh", swap_half))
    relayed = lax.ppermute(jnp.stack(own_keys + far_keys), "core", swap_core)
    blocks = [
        [own_keys[i], relayed[1 - i], far_keys[i], relayed[3 - i]] for i in range(2)
    ]
    on_second_core = lax.axis_index("core") == 1
    on_second_half = lax.axis_index("xh") == 1
    relative = []
    for k in range(replica_count):
        part = None
        for i in range(2):
            term = jnp.einsum(
                "rf,rg->fg", blocks[i][0], blocks[i][k], preferred_element_type=jnp.float32
            )
            part = term if part is None else part + term
        relative.append(with_layout_constraint(part, Layout(major_to_minor=(0, 1))))
    by_core = [jnp.where(on_second_core, relative[k ^ 1], relative[k]) for k in range(4)]
    by_half = [jnp.where(on_second_half, by_core[k ^ 2], by_core[k]) for k in range(4)]
    key_gram = jnp.concatenate(by_half, axis=1) * factor
    return key_gram[None]


def solution(mesh):
    expert_count, replica_count = mesh.devices.shape
    split = Mesh(
        mesh.devices.reshape(expert_count, 2, replica_count // 2), ("expert", "xh", "core")
    )
    rows = ("expert", "xh", "core")
    step = jax.shard_map(
        body,
        mesh=split,
        in_specs=(
            P(rows, None),
            P(rows, None),
            P(rows),
            P("expert", None, ("xh", "core")),
            P("expert", None, ("xh", "core")),
        ),
        out_specs=P("expert", ("xh", "core"), None),
        check_vma=False,
    )
    out_sharding = NamedSharding(mesh, P("expert", "replica", None))

    def run(tokens, routes, counts, w_gate, w_up):
        out = step(tokens, routes, counts, w_gate, w_up)
        return lax.with_sharding_constraint(out, out_sharding)

    return run
```

```python
import jax
import jax.numpy as jnp
from jax import lax
from jax.experimental.layout import Layout, with_layout_constraint
from jax.sharding import Mesh, NamedSharding, PartitionSpec as P

N_ROUTED = 256
TOP = 8


def slot_onehot(routes, real_count, expert_total, capacity):
    tokens_here = routes.shape[0]
    token = lax.broadcasted_iota(jnp.int32, (tokens_here, 1), 0)
    expert = lax.broadcasted_iota(jnp.int32, (1, 1, expert_total), 2)
    hit = jnp.any(routes[:, :, None] == expert, axis=1) & (token < real_count)
    row = lax.broadcasted_iota(jnp.int32, (tokens_here, tokens_here), 0)
    col = lax.broadcasted_iota(jnp.int32, (tokens_here, tokens_here), 1)
    earlier = (col < row).astype(jnp.bfloat16)
    rank = jnp.dot(earlier, hit.astype(jnp.bfloat16), preferred_element_type=jnp.float32)
    rank = rank.astype(jnp.int32)
    slot = lax.broadcasted_iota(jnp.int32, (1, capacity, 1), 1)
    return hit.T[:, None, :] & (rank.T[:, None, :] == slot)


def body(tokens, routes, counts, w_gate, w_up):
    expert_count = lax.axis_size("expert")
    half_count = lax.axis_size("xh")
    core_count = lax.axis_size("core")
    slot_total, width_model = tokens.shape
    capacity = slot_total * TOP // N_ROUTED
    onehot = slot_onehot(routes, counts[0], expert_count, capacity)
    onehot = jnp.broadcast_to(
        onehot[:, None], (expert_count, half_count, capacity, slot_total)
    ).reshape(expert_count * half_count * capacity, slot_total)
    slot_rows = jnp.dot(
        onehot.astype(tokens.dtype), tokens, preferred_element_type=jnp.float32
    ).astype(tokens.dtype)
    slot_rows = slot_rows.reshape(expert_count * half_count, capacity, width_model)
    slot_block = lax.all_to_all(
        slot_rows, ("expert", "xh"), split_axis=0, concat_axis=0, tiled=True
    )
    slot_block = slot_block.reshape(expert_count * half_count * capacity, width_model)
    partner = lax.ppermute(slot_block, "core", [(c, (c + 1) % core_count) for c in range(core_count)])
    factor = 1.0 / (expert_count * capacity)
    swap_half = [(h, (h + 1) % half_count) for h in range(half_count)]
    swap_core = [(c, (c + 1) % core_count) for c in range(core_count)]
    replica_count = half_count * core_count
    rows_half = slot_block.shape[0] // 2
    pieces = [[slot_block[:rows_half], slot_block[rows_half:]], [partner]]
    own_keys, far_keys = [], []
    for group in pieces:
        keys_here, far_here = [], []
        for rows in group:
            gate_pre = jnp.dot(rows, w_gate[0], preferred_element_type=jnp.float32)
            up_pre = jnp.dot(rows, w_up[0], preferred_element_type=jnp.float32)
            keys = (jax.nn.silu(gate_pre) * up_pre).astype(jnp.bfloat16)
            keys = with_layout_constraint(keys, Layout(major_to_minor=(0, 1)))
            keys_here.append(keys)
            far_here.append(lax.ppermute(keys, "xh", swap_half))
        own_keys.append(jnp.concatenate(keys_here, axis=0))
        far_keys.append(jnp.concatenate(far_here, axis=0))
    relayed = lax.ppermute(jnp.stack(own_keys + far_keys), "core", swap_core)
    blocks = [
        [own_keys[i], relayed[1 - i], far_keys[i], relayed[3 - i]] for i in range(2)
    ]
    on_second_core = lax.axis_index("core") == 1
    on_second_half = lax.axis_index("xh") == 1

    def absolute(rel):
        by_core = [jnp.where(on_second_core, rel[k ^ 1], rel[k]) for k in range(4)]
        by_half = [jnp.where(on_second_half, by_core[k ^ 2], by_core[k]) for k in range(4)]
        return jnp.concatenate(by_half, axis=1)

    key_gram = None
    for i in range(2):
        part = jnp.einsum(
            "rf,rg->fg", blocks[i][0], absolute(blocks[i]), preferred_element_type=jnp.float32
        )
        key_gram = part if key_gram is None else key_gram + part
    key_gram = key_gram * factor
    return key_gram[None]


def solution(mesh):
    expert_count, replica_count = mesh.devices.shape
    split = Mesh(
        mesh.devices.reshape(expert_count, 2, replica_count // 2), ("expert", "xh", "core")
    )
    rows = ("expert", "xh", "core")
    step = jax.shard_map(
        body,
        mesh=split,
        in_specs=(
            P(rows, None),
            P(rows, None),
            P(rows),
            P("expert", None, ("xh", "core")),
            P("expert", None, ("xh", "core")),
        ),
        out_specs=P("expert", ("xh", "core"), None),
        check_vma=False,
    )
    out_sharding = NamedSharding(mesh, P("expert", "replica", None))

    def run(tokens, routes, counts, w_gate, w_up):
        out = step(tokens, routes, counts, w_gate, w_up)
        return lax.with_sharding_constraint(out, out_sharding)

    return run
```

```python
import jax
import jax.numpy as jnp
from jax import lax
from jax.experimental.layout import Layout, with_layout_constraint
from jax.sharding import Mesh, NamedSharding, PartitionSpec as P

N_ROUTED = 256
TOP = 8


def slot_onehot(routes, real_count, expert_total, capacity):
    tokens_here = routes.shape[0]
    token = lax.broadcasted_iota(jnp.int32, (tokens_here, 1), 0)
    expert = lax.broadcasted_iota(jnp.int32, (1, 1, expert_total), 2)
    hit = jnp.any(routes[:, :, None] == expert, axis=1) & (token < real_count)
    row = lax.broadcasted_iota(jnp.int32, (tokens_here, tokens_here), 0)
    col = lax.broadcasted_iota(jnp.int32, (tokens_here, tokens_here), 1)
    earlier = (col < row).astype(jnp.bfloat16)
    rank = jnp.dot(earlier, hit.astype(jnp.bfloat16), preferred_element_type=jnp.float32)
    rank = rank.astype(jnp.int32)
    slot = lax.broadcasted_iota(jnp.int32, (1, capacity, 1), 1)
    return hit.T[:, None, :] & (rank.T[:, None, :] == slot)


def body(tokens, routes, counts, w_gate, w_up):
    expert_count = lax.axis_size("expert")
    half_count = lax.axis_size("xh")
    core_count = lax.axis_size("core")
    slot_total, width_model = tokens.shape
    capacity = slot_total * TOP // N_ROUTED
    onehot = slot_onehot(routes, counts[0], expert_count, capacity)
    onehot = jnp.broadcast_to(
        onehot[None], (half_count, expert_count, capacity, slot_total)
    ).reshape(half_count * expert_count * capacity, slot_total)
    slot_rows = jnp.dot(
        onehot.astype(tokens.dtype), tokens, preferred_element_type=jnp.float32
    ).astype(tokens.dtype)
    slot_rows = slot_rows.reshape(expert_count * half_count, capacity, width_model)
    slot_block = lax.all_to_all(
        slot_rows, ("xh", "expert"), split_axis=0, concat_axis=0, tiled=True
    )
    slot_block = slot_block.reshape(expert_count * half_count * capacity, width_model)
    partner = lax.ppermute(slot_block, "core", [(c, (c + 1) % core_count) for c in range(core_count)])
    factor = 1.0 / (expert_count * capacity)
    swap_half = [(h, (h + 1) % half_count) for h in range(half_count)]
    swap_core = [(c, (c + 1) % core_count) for c in range(core_count)]
    replica_count = half_count * core_count
    own_keys, far_keys = [], []
    for rows in (slot_block, partner):
        gate_pre = jnp.dot(rows, w_gate[0], preferred_element_type=jnp.float32)
        up_pre = jnp.dot(rows, w_up[0], preferred_element_type=jnp.float32)
        keys = (jax.nn.silu(gate_pre) * up_pre).astype(jnp.bfloat16)
        keys = with_layout_constraint(keys, Layout(major_to_minor=(0, 1)))
        own_keys.append(keys)
        far_keys.append(lax.ppermute(keys, "xh", swap_half))
    relayed = lax.ppermute(jnp.stack(own_keys + far_keys), "core", swap_core)
    blocks = [
        [own_keys[i], relayed[1 - i], far_keys[i], relayed[3 - i]] for i in range(2)
    ]
    on_second_core = lax.axis_index("core") == 1
    on_second_half = lax.axis_index("xh") == 1

    def absolute(rel):
        by_core = [jnp.where(on_second_core, rel[k ^ 1], rel[k]) for k in range(4)]
        by_half = [jnp.where(on_second_half, by_core[k ^ 2], by_core[k]) for k in range(4)]
        return jnp.concatenate(by_half, axis=1)

    key_gram = None
    for i in range(2):
        part = jnp.einsum(
            "rf,rg->fg", blocks[i][0], absolute(blocks[i]), preferred_element_type=jnp.float32
        )
        key_gram = part if key_gram is None else key_gram + part
    key_gram = key_gram * factor
    return key_gram[None]


def solution(mesh):
    expert_count, replica_count = mesh.devices.shape
    split = Mesh(
        mesh.devices.reshape(expert_count, 2, replica_count // 2), ("expert", "xh", "core")
    )
    rows = ("expert", "xh", "core")
    step = jax.shard_map(
        body,
        mesh=split,
        in_specs=(
            P(rows, None),
            P(rows, None),
            P(rows),
            P("expert", None, ("xh", "core")),
            P("expert", None, ("xh", "core")),
        ),
        out_specs=P("expert", ("xh", "core"), None),
        check_vma=False,
    )
    out_sharding = NamedSharding(mesh, P("expert", "replica", None))

    def run(tokens, routes, counts, w_gate, w_up):
        out = step(tokens, routes, counts, w_gate, w_up)
        return lax.with_sharding_constraint(out, out_sharding)

    return run
```

```python
import jax
import jax.numpy as jnp
from jax import lax
from jax.experimental.layout import Layout, with_layout_constraint
from jax.sharding import Mesh, NamedSharding, PartitionSpec as P

N_ROUTED = 256
TOP = 8


def slot_onehot(routes, real_count, expert_total, capacity):
    tokens_here = routes.shape[0]
    token = lax.broadcasted_iota(jnp.int32, (tokens_here, 1), 0)
    expert = lax.broadcasted_iota(jnp.int32, (1, 1, expert_total), 2)
    hit = jnp.any(routes[:, :, None] == expert, axis=1) & (token < real_count)
    row = lax.broadcasted_iota(jnp.int32, (tokens_here, tokens_here), 0)
    col = lax.broadcasted_iota(jnp.int32, (tokens_here, tokens_here), 1)
    earlier = (col < row).astype(jnp.bfloat16)
    rank = jnp.dot(earlier, hit.astype(jnp.bfloat16), preferred_element_type=jnp.float32)
    rank = rank.astype(jnp.int32)
    slot = lax.broadcasted_iota(jnp.int32, (1, capacity, 1), 1)
    return hit.T[:, None, :] & (rank.T[:, None, :] == slot)


def body(tokens, routes, counts, w_gate, w_up):
    expert_count = lax.axis_size("expert")
    half_count = lax.axis_size("xh")
    core_count = lax.axis_size("core")
    slot_total, width_model = tokens.shape
    capacity = slot_total * TOP // N_ROUTED
    onehot = slot_onehot(routes, counts[0], expert_count, capacity)
    onehot = jnp.broadcast_to(
        onehot[:, None], (expert_count, half_count, capacity, slot_total)
    ).reshape(expert_count * half_count * capacity, slot_total)
    slot_rows = jnp.dot(
        onehot.astype(tokens.dtype), tokens, preferred_element_type=jnp.float32
    ).astype(tokens.dtype)
    slot_rows = slot_rows.reshape(expert_count * half_count, capacity, width_model)
    slot_block = lax.all_to_all(
        slot_rows, ("expert", "xh"), split_axis=0, concat_axis=0, tiled=True
    )
    slot_block = slot_block.reshape(expert_count * half_count * capacity, width_model)
    rows_half = slot_block.shape[0] // 2
    partner = [
        lax.ppermute(piece, "core", [(c, (c + 1) % core_count) for c in range(core_count)])
        for piece in (slot_block[:rows_half], slot_block[rows_half:])
    ]
    factor = 1.0 / (expert_count * capacity)
    swap_half = [(h, (h + 1) % half_count) for h in range(half_count)]
    swap_core = [(c, (c + 1) % core_count) for c in range(core_count)]
    replica_count = half_count * core_count
    own_keys, far_keys = [], []
    for group in ([slot_block], partner):
        pieces = []
        for rows in group:
            gate_pre = jnp.dot(rows, w_gate[0], preferred_element_type=jnp.float32)
            up_pre = jnp.dot(rows, w_up[0], preferred_element_type=jnp.float32)
            pieces.append((jax.nn.silu(gate_pre) * up_pre).astype(jnp.bfloat16))
        keys = jnp.concatenate(pieces, axis=0)
        keys = with_layout_constraint(keys, Layout(major_to_minor=(0, 1)))
        own_keys.append(keys)
        far_keys.append(lax.ppermute(keys, "xh", swap_half))
    relayed = lax.ppermute(jnp.stack(own_keys + far_keys), "core", swap_core)
    blocks = [
        [own_keys[i], relayed[1 - i], far_keys[i], relayed[3 - i]] for i in range(2)
    ]
    on_second_core = lax.axis_index("core") == 1
    on_second_half = lax.axis_index("xh") == 1

    def absolute(rel):
        by_core = [jnp.where(on_second_core, rel[k ^ 1], rel[k]) for k in range(4)]
        by_half = [jnp.where(on_second_half, by_core[k ^ 2], by_core[k]) for k in range(4)]
        return jnp.concatenate(by_half, axis=1)

    key_gram = None
    for i in range(2):
        part = jnp.einsum(
            "rf,rg->fg", blocks[i][0], absolute(blocks[i]), preferred_element_type=jnp.float32
        )
        key_gram = part if key_gram is None else key_gram + part
    key_gram = key_gram * factor
    return key_gram[None]


def solution(mesh):
    expert_count, replica_count = mesh.devices.shape
    split = Mesh(
        mesh.devices.reshape(expert_count, 2, replica_count // 2), ("expert", "xh", "core")
    )
    rows = ("expert", "xh", "core")
    step = jax.shard_map(
        body,
        mesh=split,
        in_specs=(
            P(rows, None),
            P(rows, None),
            P(rows),
            P("expert", None, ("xh", "core")),
            P("expert", None, ("xh", "core")),
        ),
        out_specs=P("expert", ("xh", "core"), None),
        check_vma=False,
    )
    out_sharding = NamedSharding(mesh, P("expert", "replica", None))

    def run(tokens, routes, counts, w_gate, w_up):
        out = step(tokens, routes, counts, w_gate, w_up)
        return lax.with_sharding_constraint(out, out_sharding)

    return run
```

```python
import jax
import jax.numpy as jnp
from jax import lax
from jax.experimental.layout import Layout, with_layout_constraint
from jax.sharding import Mesh, NamedSharding, PartitionSpec as P

N_ROUTED = 256
TOP = 8


def slot_onehot(routes, real_count, expert_total, capacity):
    tokens_here = routes.shape[0]
    token = lax.broadcasted_iota(jnp.int32, (tokens_here, 1), 0)
    expert = lax.broadcasted_iota(jnp.int32, (1, 1, expert_total), 2)
    hit = jnp.any(routes[:, :, None] == expert, axis=1) & (token < real_count)
    row = lax.broadcasted_iota(jnp.int32, (tokens_here, tokens_here), 0)
    col = lax.broadcasted_iota(jnp.int32, (tokens_here, tokens_here), 1)
    earlier = (col < row).astype(jnp.bfloat16)
    rank = jnp.dot(earlier, hit.astype(jnp.bfloat16), preferred_element_type=jnp.float32)
    rank = rank.astype(jnp.int32)
    slot = lax.broadcasted_iota(jnp.int32, (1, capacity, 1), 1)
    return hit.T[:, None, :] & (rank.T[:, None, :] == slot)


def body(tokens, routes, counts, w_gate, w_up):
    expert_count = lax.axis_size("expert")
    half_count = lax.axis_size("xh")
    core_count = lax.axis_size("core")
    slot_total, width_model = tokens.shape
    capacity = slot_total * TOP // N_ROUTED
    onehot = slot_onehot(routes, counts[0], expert_count, capacity)
    onehot = jnp.broadcast_to(
        onehot[:, None], (expert_count, half_count, capacity, slot_total)
    ).reshape(expert_count * half_count * capacity, slot_total)
    slot_rows = jnp.dot(
        onehot.astype(tokens.dtype), tokens, preferred_element_type=jnp.float32
    ).astype(tokens.dtype)
    slot_rows = slot_rows.reshape(expert_count * half_count, capacity, width_model)
    slot_block = lax.all_to_all(
        slot_rows, ("expert", "xh"), split_axis=0, concat_axis=0, tiled=True
    )
    slot_block = slot_block.reshape(expert_count * half_count * capacity, width_model)
    partner = lax.ppermute(slot_block, "core", [(c, (c + 1) % core_count) for c in range(core_count)])
    factor = 1.0 / (expert_count * capacity)
    swap_half = [(h, (h + 1) % half_count) for h in range(half_count)]
    swap_core = [(c, (c + 1) % core_count) for c in range(core_count)]
    replica_count = half_count * core_count
    own_keys, far_keys = [], []
    for rows in (slot_block, partner):
        gate_pre = jnp.dot(rows, w_gate[0], preferred_element_type=jnp.float32)
        up_pre = jnp.dot(rows, w_up[0], preferred_element_type=jnp.float32)
        keys = (jax.nn.silu(gate_pre) * up_pre).astype(jnp.bfloat16)
        keys = with_layout_constraint(keys, Layout(major_to_minor=(0, 1)))
        own_keys.append(keys)
        far_keys.append(lax.ppermute(keys, "xh", swap_half))
    relayed = [
        lax.ppermute(jnp.stack([own_keys[i], far_keys[i]]), "core", swap_core) for i in range(2)
    ]
    blocks = [
        [own_keys[i], relayed[1 - i][0], far_keys[i], relayed[1 - i][1]] for i in range(2)
    ]
    on_second_core = lax.axis_index("core") == 1
    on_second_half = lax.axis_index("xh") == 1

    def absolute(rel):
        by_core = [jnp.where(on_second_core, rel[k ^ 1], rel[k]) for k in range(4)]
        by_half = [jnp.where(on_second_half, by_core[k ^ 2], by_core[k]) for k in range(4)]
        return jnp.concatenate(by_half, axis=1)

    key_gram = None
    for i in range(2):
        part = jnp.einsum(
            "rf,rg->fg", blocks[i][0], absolute(blocks[i]), preferred_element_type=jnp.float32
        )
        key_gram = part if key_gram is None else key_gram + part
    key_gram = key_gram * factor
    return key_gram[None]


def solution(mesh):
    expert_count, replica_count = mesh.devices.shape
    split = Mesh(
        mesh.devices.reshape(expert_count, 2, replica_count // 2), ("expert", "xh", "core")
    )
    rows = ("expert", "xh", "core")
    step = jax.shard_map(
        body,
        mesh=split,
        in_specs=(
            P(rows, None),
            P(rows, None),
            P(rows),
            P("expert", None, ("xh", "core")),
            P("expert", None, ("xh", "core")),
        ),
        out_specs=P("expert", ("xh", "core"), None),
        check_vma=False,
    )
    out_sharding = NamedSharding(mesh, P("expert", "replica", None))

    def run(tokens, routes, counts, w_gate, w_up):
        out = step(tokens, routes, counts, w_gate, w_up)
        return lax.with_sharding_constraint(out, out_sharding)

    return run
```

```python
import jax
import jax.numpy as jnp
from jax import lax
from jax.experimental.layout import Layout, with_layout_constraint
from jax.sharding import Mesh, NamedSharding, PartitionSpec as P

N_ROUTED = 256
TOP = 8


def slot_onehot(routes, real_count, expert_total, capacity):
    tokens_here = routes.shape[0]
    token = lax.broadcasted_iota(jnp.int32, (tokens_here, 1), 0)
    expert = lax.broadcasted_iota(jnp.int32, (1, 1, expert_total), 2)
    hit = jnp.any(routes[:, :, None] == expert, axis=1) & (token < real_count)
    row = lax.broadcasted_iota(jnp.int32, (tokens_here, tokens_here), 0)
    col = lax.broadcasted_iota(jnp.int32, (tokens_here, tokens_here), 1)
    earlier = (col < row).astype(jnp.bfloat16)
    rank = jnp.dot(earlier, hit.astype(jnp.bfloat16), preferred_element_type=jnp.float32)
    rank = rank.astype(jnp.int32)
    slot = lax.broadcasted_iota(jnp.int32, (1, capacity, 1), 1)
    return hit.T[:, None, :] & (rank.T[:, None, :] == slot)


def body(tokens, routes, counts, w_gate, w_up):
    expert_count = lax.axis_size("expert")
    half_count = lax.axis_size("xh")
    core_count = lax.axis_size("core")
    slot_total, width_model = tokens.shape
    capacity = slot_total * TOP // N_ROUTED
    onehot = slot_onehot(routes, counts[0], expert_count, capacity)
    slot_rows = jnp.dot(
        onehot.reshape(expert_count * capacity, slot_total).astype(tokens.dtype),
        tokens,
        preferred_element_type=jnp.float32,
    ).astype(tokens.dtype)
    slot_rows = jnp.broadcast_to(
        slot_rows.reshape(expert_count, 1, capacity, width_model),
        (expert_count, half_count, capacity, width_model),
    ).reshape(expert_count * half_count, capacity, width_model)
    slot_block = lax.all_to_all(
        slot_rows, ("expert", "xh"), split_axis=0, concat_axis=0, tiled=True
    )
    slot_block = slot_block.reshape(expert_count * half_count * capacity, width_model)
    partner = lax.ppermute(slot_block, "core", [(c, (c + 1) % core_count) for c in range(core_count)])
    factor = 1.0 / (expert_count * capacity)
    swap_half = [(h, (h + 1) % half_count) for h in range(half_count)]
    swap_core = [(c, (c + 1) % core_count) for c in range(core_count)]
    replica_count = half_count * core_count
    own_keys, far_keys = [], []
    for rows in (slot_block, partner):
        gate_pre = jnp.dot(rows, w_gate[0], preferred_element_type=jnp.float32)
        up_pre = jnp.dot(rows, w_up[0], preferred_element_type=jnp.float32)
        keys = (jax.nn.silu(gate_pre) * up_pre).astype(jnp.bfloat16)
        keys = with_layout_constraint(keys, Layout(major_to_minor=(0, 1)))
        own_keys.append(keys)
        far_keys.append(lax.ppermute(keys, "xh", swap_half))
    relayed = lax.ppermute(jnp.stack(own_keys + far_keys), "core", swap_core)
    blocks = [
        [own_keys[i], relayed[1 - i], far_keys[i], relayed[3 - i]] for i in range(2)
    ]
    on_second_core = lax.axis_index("core") == 1
    on_second_half = lax.axis_index("xh") == 1

    def absolute(rel):
        by_core = [jnp.where(on_second_core, rel[k ^ 1], rel[k]) for k in range(4)]
        by_half = [jnp.where(on_second_half, by_core[k ^ 2], by_core[k]) for k in range(4)]
        return jnp.concatenate(by_half, axis=1)

    key_gram = None
    for i in range(2):
        part = jnp.einsum(
            "rf,rg->fg", blocks[i][0], absolute(blocks[i]), preferred_element_type=jnp.float32
        )
        key_gram = part if key_gram is None else key_gram + part
    key_gram = key_gram * factor
    return key_gram[None]


def solution(mesh):
    expert_count, replica_count = mesh.devices.shape
    split = Mesh(
        mesh.devices.reshape(expert_count, 2, replica_count // 2), ("expert", "xh", "core")
    )
    rows = ("expert", "xh", "core")
    step = jax.shard_map(
        body,
        mesh=split,
        in_specs=(
            P(rows, None),
            P(rows, None),
            P(rows),
            P("expert", None, ("xh", "core")),
            P("expert", None, ("xh", "core")),
        ),
        out_specs=P("expert", ("xh", "core"), None),
        check_vma=False,
    )
    out_sharding = NamedSharding(mesh, P("expert", "replica", None))

    def run(tokens, routes, counts, w_gate, w_up):
        out = step(tokens, routes, counts, w_gate, w_up)
        return lax.with_sharding_constraint(out, out_sharding)

    return run
```
